128 devices in a mesh: tm: 4 (over y_hi, core), row: 8 (over y_lo, z), col: 4 (over x).
Axes of the slice: x: 4, y: 4 (y_hi: 2, y_lo: 2; y = y_hi * 2 + y_lo), z: 4, core: 2. Of those that a mesh axis runs over, the one named last changes fastest.
Arguments:
- latent: bfloat16 [16, 64, 32, 256], P('tm', 'row', 'col'), may hold values from -6 to 6
- w_first: bfloat16 [3, 3, 3, 256, 256], replicated, may hold values from -0.078125 to 0.078125
- b_first: float32 [256], replicated, may hold values from -3 to 3
- w_second: bfloat16 [3, 3, 3, 256, 256], replicated, may hold values from -0.078125 to 0.078125
- b_second: float32 [256], replicated, may hold values from -3 to 3
- upstream: bfloat16 [16, 128, 64, 256], P('tm', 'row', 'col'), may hold values from -6 to 6
- dropout_key: int32 [2], replicated, may hold values from 0 to 1073741823
Outputs:
- mixed: bfloat16 [16, 128, 64, 256], P('tm', 'row', 'col')
- grad_latent: bfloat16 [16, 64, 32, 256], P('tm', 'row', 'col')
- grad_first: float32 [3, 3, 3, 256, 256], replicated
- grad_second: float32 [3, 3, 3, 256, 256], replicated
The draws below stay inside these ranges and needn't reach their ends.
All inputs are finite; a program needn't handle non-finite values.
Results may differ from the reference program's by a relative error of at most 0.0032.
Values may be sent and summed in bfloat16 or wider, within the bound.
No kernel may reach another device: no remote copies, remote signals or barrier semaphores. Data moves between devices by JAX's collectives and lax.ppermute only.
A program may use at most 128 MiB of HBM per device.

```python
import jax
import jax.numpy as jnp
from jax import lax

C = 256
FRAMES = 16
LH = 64
LW = 32
HH = 128
HW = 64


def shard_levels(rng, dims, split, least, top_value):
    loudness, own = 1.0, jax.random.fold_in(rng, 6)
    for position, blocks in split:
        draws = jnp.exp(jax.random.uniform(jax.random.fold_in(own, position), (blocks,), jnp.float32, least / len(split), top_value / len(split)))
        loudness = loudness * jnp.repeat(draws, dims[position] // blocks).reshape([-1 if axis == position else 1 for axis in range(len(dims))])
    return loudness


def bell_draw(own_key, extent, spread, reach, shards=(), dtype=jnp.bfloat16):
    array = spread * jax.random.normal(own_key, extent, jnp.float32)
    if shards:
        array = array * shard_levels(own_key, extent, shards, -0.22, 0.18)
    return jnp.clip(array, -reach, reach).astype(dtype)


def setup_inputs(seed: int = 0) -> dict:
    key_list = jax.random.split(jax.random.key(seed), 8)
    return {
        "latent": bell_draw(key_list[0], (FRAMES, LH, LW, C), 1.0, 6.0, ((0, 4), (1, 8), (2, 4))),
        "w_first": bell_draw(key_list[1], (3, 3, 3, C, C), (27 * C) ** -0.5, 0.078125),
        "b_first": bell_draw(key_list[2], (C,), 0.5, 3.0, (), jnp.float32),
        "w_second": bell_draw(key_list[3], (3, 3, 3, C, C), (27 * C) ** -0.5, 0.078125),
        "b_second": bell_draw(key_list[4], (C,), 0.5, 3.0, (), jnp.float32),
        "upstream": bell_draw(key_list[5], (FRAMES, HH, HW, C), 1.0, 6.0, ((0, 4), (1, 8), (2, 4))),
        "dropout_key": jax.random.randint(key_list[6], (2,), 0, 1073741824).astype(jnp.int32),
    }


KEEP_LEVEL = 6554
KEEP_SCALE = 65536.0 / 58982.0


def keep_mask(dropout_key, frame_start, row_start, col_start, shape, height_all, width_all):
    frame_idx = lax.broadcasted_iota(jnp.int32, shape, 0) + frame_start
    row_idx = lax.broadcasted_iota(jnp.int32, shape, 1) + row_start
    col_idx = lax.broadcasted_iota(jnp.int32, shape, 2) + col_start
    chan_idx = lax.broadcasted_iota(jnp.int32, shape, 3)
    linear = ((frame_idx * height_all + row_idx) * width_all + col_idx) * shape[3] + chan_idx
    state = linear * jnp.int32(-1640531535) + dropout_key[0]
    state = state ^ lax.shift_right_logical(state, jnp.full(shape, 16, jnp.int32))
    state = state * jnp.int32(-2048144789) + dropout_key[1]
    state = state ^ lax.shift_right_logical(state, jnp.full(shape, 13, jnp.int32))
    state = state * jnp.int32(-1028477387)
    state = state ^ lax.shift_right_logical(state, jnp.full(shape, 16, jnp.int32))
    kept = (state & 65535) >= KEEP_LEVEL
    return jnp.where(kept, jnp.float32(KEEP_SCALE), jnp.float32(0.0)).astype(jnp.float32)


def upsample(field):
    return jnp.repeat(jnp.repeat(field, 2, axis=1), 2, axis=2)


def unfold(extended):
    frames_out = extended.shape[0] - 2
    height = extended.shape[1] - 2
    width = extended.shape[2] - 2
    pieces = [extended[a:a + frames_out, b:b + height, c:c + width] for a in range(3) for b in range(3) for c in range(3)]
    return jnp.concatenate(pieces, axis=-1).reshape(frames_out * height * width, -1)


def convolve(patches, weight, shape):
    matrix = weight.reshape(-1, weight.shape[-1])
    return jnp.dot(patches, matrix, preferred_element_type=jnp.float32).reshape(shape)


def flipped(weight):
    return jnp.swapaxes(weight[::-1, ::-1, ::-1], 3, 4)


def weight_gradient(patches, grad):
    channels = grad.shape[-1]
    summed = lax.dot_general(patches, grad.reshape(-1, channels), (((0,), (0,)), ((), ())), preferred_element_type=jnp.float32)
    return summed.reshape(3, 3, 3, channels, channels)


def conv_frames(extended, weight):
    frames_out = extended.shape[0] - 2
    shape = (1, extended.shape[1] - 2, extended.shape[2] - 2, weight.shape[-1])
    outputs = [convolve(unfold(extended[t:t + 3]), weight, shape) for t in range(frames_out)]
    return jnp.concatenate(outputs, axis=0)


def grad_frames(extended, grad):
    summed = jnp.zeros((3, 3, 3, grad.shape[-1], grad.shape[-1]), jnp.float32)
    for t in range(grad.shape[0]):
        summed = summed + weight_gradient(unfold(extended[t:t + 3]), grad[t:t + 1])
    return summed


def reference(latent, w_first, b_first, w_second, b_second, upstream, dropout_key):
    cells = upsample(latent)
    shape = cells.shape
    earlier_pad = ((2, 0), (1, 1), (1, 1), (0, 0))
    later_pad = ((0, 2), (1, 1), (1, 1), (0, 0))
    cells_ext = jnp.pad(cells, earlier_pad)
    pre_first = conv_frames(cells_ext, w_first) + b_first
    scaling = keep_mask(dropout_key, jnp.int32(0), jnp.int32(0), jnp.int32(0), shape, shape[1], shape[2])
    dropped = (jax.nn.silu(pre_first) * scaling).astype(jnp.bfloat16)
    dropped_ext = jnp.pad(dropped, earlier_pad)
    mixed = (cells.astype(jnp.float32) + conv_frames(dropped_ext, w_second) + b_second).astype(jnp.bfloat16)
    grad_dropped = conv_frames(jnp.pad(upstream, later_pad), flipped(w_second))
    grad_second = grad_frames(dropped_ext, upstream)
    sigma = jax.nn.sigmoid(pre_first)
    grad_pre = (grad_dropped * scaling * sigma * (1.0 + pre_first * (1.0 - sigma))).astype(jnp.bfloat16)
    grad_first = grad_frames(cells_ext, grad_pre)
    grad_cells = upstream.astype(jnp.float32) + conv_frames(jnp.pad(grad_pre, later_pad), flipped(w_first))
    frames_all, low_rows, low_cols, channels = latent.shape
    grad_latent = grad_cells.reshape(frames_all, low_rows, 2, low_cols, 2, channels).sum(axis=(2, 4)).astype(jnp.bfloat16)
    return mixed, grad_latent, grad_first, grad_second
```

```python
import jax
import jax.numpy as jnp
from jax import lax
from jax.sharding import PartitionSpec as P

KEEP_LEVEL = 6554
KEEP_SCALE = 65536.0 / 58982.0
ALL = ("tm", "row", "col")


def shifted(block, axis, distance):
    devices = range(lax.axis_size(axis))
    route = [(i - distance, i) for i in devices if i - distance in devices]
    return lax.ppermute(block, axis, route)


def extended_2(cells, sides, width):
    for axis, dim in sides:
        count = lax.axis_size(axis)
        ends = count - 1
        head = lax.slice_in_dim(cells, 0, width, axis=dim)
        tail = lax.slice_in_dim(cells, cells.shape[dim] - width, cells.shape[dim], axis=dim)
        cells = jnp.concatenate(
            [
                lax.ppermute(tail, axis, [(i, (i + 1) % count) for i in range(ends)]),
                cells,
                lax.ppermute(head, axis, [((i + 1) % count, i) for i in range(ends)]),
            ],
            axis=dim,
        )
    return cells


def keep_mask(dropout_key, frame_start, row_start, col_start, shape, height_all, width_all):
    frame_idx = lax.broadcasted_iota(jnp.int32, shape, 0) + frame_start
    row_idx = lax.broadcasted_iota(jnp.int32, shape, 1) + row_start
    col_idx = lax.broadcasted_iota(jnp.int32, shape, 2) + col_start
    chan_idx = lax.broadcasted_iota(jnp.int32, shape, 3)
    linear = ((frame_idx * height_all + row_idx) * width_all + col_idx) * shape[3] + chan_idx
    state = linear * jnp.int32(-1640531535) + dropout_key[0]
    state = state ^ lax.shift_right_logical(state, jnp.full(shape, 16, jnp.int32))
    state = state * jnp.int32(-2048144789) + dropout_key[1]
    state = state ^ lax.shift_right_logical(state, jnp.full(shape, 13, jnp.int32))
    state = state * jnp.int32(-1028477387)
    state = state ^ lax.shift_right_logical(state, jnp.full(shape, 16, jnp.int32))
    kept = state & 65535 >= KEEP_LEVEL
    return jnp.where(kept, jnp.float32(KEEP_SCALE), jnp.float32(0.0))


def upsample(field):
    return jnp.repeat(jnp.repeat(field, 2, axis=1), 2, axis=2)


def convolve(extended, weight):
    return lax.conv_general_dilated(
        extended[None],
        weight,
        (1, 1, 1),
        "VALID",
        dimension_numbers=("NDHWC", "DHWIO", "NDHWC"),
        preferred_element_type=jnp.float32,
    )[0]


def flipped(weight):
    return jnp.swapaxes(weight[::-1, ::-1, ::-1], 3, 4)


def weight_gradient(extended, grad):
    summed = lax.conv_general_dilated(
        extended[None],
        grad[None],
        (1, 1, 1),
        "VALID",
        dimension_numbers=("CDHWN", "IDHWO", "NDHWC"),
        preferred_element_type=jnp.float32,
    )
    return jnp.transpose(summed, (1, 2, 3, 0, 4))


def reduced(grad):
    count = 8
    for axis in ALL:
        count *= lax.axis_size(axis)
    flat = grad.reshape(-1, grad.shape[-1])
    rows = flat.shape[0]
    padded = -(-rows // count) * count
    flat = jnp.pad(flat, ((0, padded - rows), (0, 0)))
    for axis in ALL:
        flat = lax.psum_scatter(flat, axis, scatter_dimension=0, tiled=True)
    flat = flat.astype(jnp.bfloat16)
    for axis in ALL[::-1]:
        flat = lax.all_gather(flat, axis, axis=0, tiled=True)
    return flat[:rows].astype(jnp.float32).reshape(grad.shape)


def with_earlier(field):
    frames_here = field.shape[0]
    tail = shifted(field[frames_here - 2 :], "tm", 1)
    return jnp.concatenate([tail, field], axis=0)


def with_later(field):
    head = shifted(field[:2], "tm", -1)
    return jnp.concatenate([field, head], axis=0)


def face_cells(field):
    return extended_2(field, (("row", 1), ("col", 2)), 1)


def local(latent, w_first, b_first, w_second, b_second, upstream, dropout_key):
    frames_here, low_rows, low_cols, channels = latent.shape
    high_rows = 2 * low_rows
    high_cols = 2 * low_cols
    cell_shape = (frames_here, high_rows, high_cols, channels)
    frame_start = lax.axis_index("tm") * frames_here
    row_start = lax.axis_index("row") * high_rows
    col_start = lax.axis_index("col") * high_cols
    height_all = high_rows * lax.axis_size("row")
    width_all = high_cols * lax.axis_size("col")
    latent_ext = with_earlier(latent)
    cells_ext = face_cells(upsample(latent_ext))
    cells_here = cells_ext[2:, 1:-1, 1:-1]
    pre_first = convolve(cells_ext, w_first) + b_first
    scaling = keep_mask(
        dropout_key, frame_start, row_start, col_start, cell_shape, height_all, width_all
    )
    dropped = (jax.nn.silu(pre_first) * scaling).astype(jnp.bfloat16)
    dropped_ext = face_cells(with_earlier(dropped))
    grad_second = reduced(weight_gradient(dropped_ext, upstream))
    mixed = (cells_here.astype(jnp.float32) + convolve(dropped_ext, w_second) + b_second).astype(
        jnp.bfloat16
    )
    grad_dropped = convolve(face_cells(with_later(upstream)), flipped(w_second))
    sigma = jax.nn.sigmoid(pre_first)
    grad_pre = (grad_dropped * scaling * sigma * (1.0 + pre_first * (1.0 - sigma))).astype(
        jnp.bfloat16
    )
    grad_first = reduced(weight_gradient(cells_ext, grad_pre))
    grad_cells = upstream.astype(jnp.float32) + convolve(
        face_cells(with_later(grad_pre)), flipped(w_first)
    )
    grad_latent = (
        grad_cells.reshape(frames_here, low_rows, 2, low_cols, 2, channels)
        .sum(axis=(2, 4))
        .astype(jnp.bfloat16)
    )
    return (mixed, grad_latent, grad_first, grad_second)


def solution(mesh):
    placed = (P("tm", "row", "col", None), P(), P(), P(), P(), P("tm", "row", "col", None), P())
    return jax.shard_map(
        local,
        mesh=mesh,
        in_specs=placed,
        out_specs=(P("tm", "row", "col", None), P("tm", "row", "col", None), P(), P()),
        check_vma=False,
    )
```

```python
import jax
import jax.numpy as jnp
from jax import lax
from jax.sharding import PartitionSpec as P

KEEP_LEVEL = 6554
KEEP_SCALE = 65536.0 / 58982.0
ALL = ("tm", "row", "col")


def shifted(block, axis, distance):
    devices = range(lax.axis_size(axis))
    route = [(i - distance, i) for i in devices if i - distance in devices]
    return lax.ppermute(block, axis, route)


def extended_2(cells, sides, width):
    for axis, dim in sides:
        count = lax.axis_size(axis)
        ends = count - 1
        head = lax.slice_in_dim(cells, 0, width, axis=dim)
        tail = lax.slice_in_dim(cells, cells.shape[dim] - width, cells.shape[dim], axis=dim)
        cells = jnp.concatenate(
            [
                lax.ppermute(tail, axis, [(i, (i + 1) % count) for i in range(ends)]),
                cells,
                lax.ppermute(head, axis, [((i + 1) % count, i) for i in range(ends)]),
            ],
            axis=dim,
        )
    return cells


def keep_mask(dropout_key, frame_start, row_start, col_start, shape, height_all, width_all):
    frame_idx = lax.broadcasted_iota(jnp.int32, shape, 0) + frame_start
    row_idx = lax.broadcasted_iota(jnp.int32, shape, 1) + row_start
    col_idx = lax.broadcasted_iota(jnp.int32, shape, 2) + col_start
    chan_idx = lax.broadcasted_iota(jnp.int32, shape, 3)
    linear = ((frame_idx * height_all + row_idx) * width_all + col_idx) * shape[3] + chan_idx
    state = linear * jnp.int32(-1640531535) + dropout_key[0]
    state = state ^ lax.shift_right_logical(state, jnp.full(shape, 16, jnp.int32))
    state = state * jnp.int32(-2048144789) + dropout_key[1]
    state = state ^ lax.shift_right_logical(state, jnp.full(shape, 13, jnp.int32))
    state = state * jnp.int32(-1028477387)
    state = state ^ lax.shift_right_logical(state, jnp.full(shape, 16, jnp.int32))
    kept = state & 65535 >= KEEP_LEVEL
    return jnp.where(kept, jnp.float32(KEEP_SCALE), jnp.float32(0.0))


def upsample(field):
    return jnp.repeat(jnp.repeat(field, 2, axis=1), 2, axis=2)


def convolve(extended, weight):
    return lax.conv_general_dilated(
        extended[None],
        weight,
        (1, 1, 1),
        "VALID",
        dimension_numbers=("NDHWC", "DHWIO", "NDHWC"),
        preferred_element_type=jnp.float32,
    )[0]


def flipped(weight):
    return jnp.swapaxes(weight[::-1, ::-1, ::-1], 3, 4)


def weight_gradient(extended, grad):
    summed = lax.conv_general_dilated(
        extended[None],
        grad[None],
        (1, 1, 1),
        "VALID",
        dimension_numbers=("CDHWN", "IDHWO", "NDHWC"),
        preferred_element_type=jnp.float32,
    )
    return jnp.transpose(summed, (1, 2, 3, 0, 4))


def reduced(grad, axes=ALL):
    return lax.psum(grad, axes)


def with_earlier(field):
    frames_here = field.shape[0]
    tail = shifted(field[frames_here - 2 :], "tm", 1)
    return jnp.concatenate([tail, field], axis=0)


def with_later(field):
    head = shifted(field[:2], "tm", -1)
    return jnp.concatenate([field, head], axis=0)


def face_cells(field):
    return extended_2(field, (("row", 1), ("col", 2)), 1)


def local(latent, w_first, b_first, w_second, b_second, upstream, dropout_key):
    frames_here, low_rows, low_cols, channels = latent.shape
    high_rows = 2 * low_rows
    high_cols = 2 * low_cols
    cell_shape = (frames_here, high_rows, high_cols, channels)
    frame_start = lax.axis_index("tm") * frames_here
    row_start = lax.axis_index("row") * high_rows
    col_start = lax.axis_index("col") * high_cols
    height_all = high_rows * lax.axis_size("row")
    width_all = high_cols * lax.axis_size("col")
    latent_ext = with_earlier(latent)
    cells_ext = face_cells(upsample(latent_ext))
    cells_here = cells_ext[2:, 1:-1, 1:-1]
    pre_first = convolve(cells_ext, w_first) + b_first
    scaling = keep_mask(
        dropout_key, frame_start, row_start, col_start, cell_shape, height_all, width_all
    )
    dropped = (jax.nn.silu(pre_first) * scaling).astype(jnp.bfloat16)
    dropped_ext = face_cells(with_earlier(dropped))
    grad_second = reduced(weight_gradient(dropped_ext, upstream))
    mixed = (cells_here.astype(jnp.float32) + convolve(dropped_ext, w_second) + b_second).astype(
        jnp.bfloat16
    )
    grad_dropped = convolve(face_cells(with_later(upstream)), flipped(w_second))
    sigma = jax.nn.sigmoid(pre_first)
    grad_pre = (grad_dropped * scaling * sigma * (1.0 + pre_first * (1.0 - sigma))).astype(
        jnp.bfloat16
    )
    grad_first = reduced(weight_gradient(cells_ext, grad_pre), ALL[::-1])
    grad_cells = upstream.astype(jnp.float32) + convolve(
        face_cells(with_later(grad_pre)), flipped(w_first)
    )
    grad_latent = (
        grad_cells.reshape(frames_here, low_rows, 2, low_cols, 2, channels)
        .sum(axis=(2, 4))
        .astype(jnp.bfloat16)
    )
    return (mixed, grad_latent, grad_first, grad_second)


def solution(mesh):
    placed = (P("tm", "row", "col", None), P(), P(), P(), P(), P("tm", "row", "col", None), P())
    return jax.shard_map(
        local,
        mesh=mesh,
        in_specs=placed,
        out_specs=(P("tm", "row", "col", None), P("tm", "row", "col", None), P(), P()),
        check_vma=False,
    )
```

```python
import jax
import jax.numpy as jnp
from jax import lax
from jax.sharding import PartitionSpec as P

KEEP_LEVEL = 6554
KEEP_SCALE = 65536.0 / 58982.0
ALL = ("tm", "row", "col")


def shifted(block, axis, distance):
    devices = range(lax.axis_size(axis))
    route = [(i - distance, i) for i in devices if i - distance in devices]
    return lax.ppermute(block, axis, route)


def extended_2(cells, sides, width):
    for axis, dim in sides:
        count = lax.axis_size(axis)
        ends = count - 1
        head = lax.slice_in_dim(cells, 0, width, axis=dim)
        tail = lax.slice_in_dim(cells, cells.shape[dim] - width, cells.shape[dim], axis=dim)
        cells = jnp.concatenate(
            [
                lax.ppermute(tail, axis, [(i, (i + 1) % count) for i in range(ends)]),
                cells,
                lax.ppermute(head, axis, [((i + 1) % count, i) for i in range(ends)]),
            ],
            axis=dim,
        )
    return cells


def keep_mask(dropout_key, frame_start, row_start, col_start, shape, height_all, width_all):
    frame_idx = lax.broadcasted_iota(jnp.int32, shape, 0) + frame_start
    row_idx = lax.broadcasted_iota(jnp.int32, shape, 1) + row_start
    col_idx = lax.broadcasted_iota(jnp.int32, shape, 2) + col_start
    chan_idx = lax.broadcasted_iota(jnp.int32, shape, 3)
    linear = ((frame_idx * height_all + row_idx) * width_all + col_idx) * shape[3] + chan_idx
    state = linear * jnp.int32(-1640531535) + dropout_key[0]
    state = state ^ lax.shift_right_logical(state, jnp.full(shape, 16, jnp.int32))
    state = state * jnp.int32(-2048144789) + dropout_key[1]
    state = state ^ lax.shift_right_logical(state, jnp.full(shape, 13, jnp.int32))
    state = state * jnp.int32(-1028477387)
    state = state ^ lax.shift_right_logical(state, jnp.full(shape, 16, jnp.int32))
    kept = state & 65535 >= KEEP_LEVEL
    return jnp.where(kept, jnp.float32(KEEP_SCALE), jnp.float32(0.0))


def upsample(field):
    return jnp.repeat(jnp.repeat(field, 2, axis=1), 2, axis=2)


def convolve(extended, weight):
    return lax.conv_general_dilated(
        extended[None],
        weight,
        (1, 1, 1),
        "VALID",
        dimension_numbers=("NDHWC", "DHWIO", "NDHWC"),
        preferred_element_type=jnp.float32,
    )[0]


def flipped(weight):
    return jnp.swapaxes(weight[::-1, ::-1, ::-1], 3, 4)


def weight_gradient(extended, grad):
    summed = lax.conv_general_dilated(
        extended[None],
        grad[None],
        (1, 1, 1),
        "VALID",
        dimension_numbers=("CDHWN", "IDHWO", "NDHWC"),
        preferred_element_type=jnp.float32,
    )
    return jnp.transpose(summed, (1, 2, 3, 0, 4))


def with_earlier(field):
    frames_here = field.shape[0]
    tail = shifted(field[frames_here - 2 :], "tm", 1)
    return jnp.concatenate([tail, field], axis=0)


def with_later(field):
    head = shifted(field[:2], "tm", -1)
    return jnp.concatenate([field, head], axis=0)


def face_cells(field):
    return extended_2(field, (("row", 1), ("col", 2)), 1)


def local(latent, w_first, b_first, w_second, b_second, upstream, dropout_key):
    frames_here, low_rows, low_cols, channels = latent.shape
    high_rows = 2 * low_rows
    high_cols = 2 * low_cols
    cell_shape = (frames_here, high_rows, high_cols, channels)
    frame_start = lax.axis_index("tm") * frames_here
    row_start = lax.axis_index("row") * high_rows
    col_start = lax.axis_index("col") * high_cols
    height_all = high_rows * lax.axis_size("row")
    width_all = high_cols * lax.axis_size("col")
    latent_ext = with_earlier(latent)
    cells_ext = face_cells(upsample(latent_ext))
    cells_here = cells_ext[2:, 1:-1, 1:-1]
    pre_first = convolve(cells_ext, w_first) + b_first
    scaling = keep_mask(
        dropout_key, frame_start, row_start, col_start, cell_shape, height_all, width_all
    )
    dropped = (jax.nn.silu(pre_first) * scaling).astype(jnp.bfloat16)
    dropped_ext = face_cells(with_earlier(dropped))
    grad_second = weight_gradient(dropped_ext, upstream)
    mixed = (cells_here.astype(jnp.float32) + convolve(dropped_ext, w_second) + b_second).astype(
        jnp.bfloat16
    )
    grad_dropped = convolve(face_cells(with_later(upstream)), flipped(w_second))
    sigma = jax.nn.sigmoid(pre_first)
    grad_pre = (grad_dropped * scaling * sigma * (1.0 + pre_first * (1.0 - sigma))).astype(
        jnp.bfloat16
    )
    grad_first = weight_gradient(cells_ext, grad_pre)
    grad_cells = upstream.astype(jnp.float32) + convolve(
        face_cells(with_later(grad_pre)), flipped(w_first)
    )
    grad_latent = (
        grad_cells.reshape(frames_here, low_rows, 2, low_cols, 2, channels)
        .sum(axis=(2, 4))
        .astype(jnp.bfloat16)
    )
    grad_first, grad_second = lax.psum((grad_first, grad_second), ALL)
    return (mixed, grad_latent, grad_first, grad_second)


def solution(mesh):
    placed = (P("tm", "row", "col", None), P(), P(), P(), P(), P("tm", "row", "col", None), P())
    return jax.shard_map(
        local,
        mesh=mesh,
        in_specs=placed,
        out_specs=(P("tm", "row", "col", None), P("tm", "row", "col", None), P(), P()),
        check_vma=False,
    )
```

```python
import jax
import jax.numpy as jnp
from jax import lax
from jax.sharding import PartitionSpec as P

KEEP_LEVEL = 6554
KEEP_SCALE = 65536.0 / 58982.0
ALL = ("tm", "row", "col")


def shifted(block, axis, distance):
    devices = range(lax.axis_size(axis))
    route = [(i - distance, i) for i in devices if i - distance in devices]
    return lax.ppermute(block, axis, route)


def extended_2(cells, sides, width):
    for axis, dim in sides:
        count = lax.axis_size(axis)
        ends = count - 1
        head = lax.slice_in_dim(cells, 0, width, axis=dim)
        tail = lax.slice_in_dim(cells, cells.shape[dim] - width, cells.shape[dim], axis=dim)
        cells = jnp.concatenate(
            [
                lax.ppermute(tail, axis, [(i, (i + 1) % count) for i in range(ends)]),
                cells,
                lax.ppermute(head, axis, [((i + 1) % count, i) for i in range(ends)]),
            ],
            axis=dim,
        )
    return cells


def keep_mask(dropout_key, frame_start, row_start, col_start, shape, height_all, width_all):
    frame_idx = lax.broadcasted_iota(jnp.int32, shape, 0) + frame_start
    row_idx = lax.broadcasted_iota(jnp.int32, shape, 1) + row_start
    col_idx = lax.broadcasted_iota(jnp.int32, shape, 2) + col_start
    chan_idx = lax.broadcasted_iota(jnp.int32, shape, 3)
    linear = ((frame_idx * height_all + row_idx) * width_all + col_idx) * shape[3] + chan_idx
    state = linear * jnp.int32(-1640531535) + dropout_key[0]
    state = state ^ lax.shift_right_logical(state, jnp.full(shape, 16, jnp.int32))
    state = state * jnp.int32(-2048144789) + dropout_key[1]
    state = state ^ lax.shift_right_logical(state, jnp.full(shape, 13, jnp.int32))
    state = state * jnp.int32(-1028477387)
    state = state ^ lax.shift_right_logical(state, jnp.full(shape, 16, jnp.int32))
    kept = state & 65535 >= KEEP_LEVEL
    return jnp.where(kept, jnp.float32(KEEP_SCALE), jnp.float32(0.0))


def upsample(field):
    return jnp.repeat(jnp.repeat(field, 2, axis=1), 2, axis=2)


def convolve(extended, weight):
    return lax.conv_general_dilated(
        extended[None],
        weight,
        (1, 1, 1),
        "VALID",
        dimension_numbers=("NDHWC", "DHWIO", "NDHWC"),
        preferred_element_type=jnp.float32,
    )[0]


def flipped(weight):
    return jnp.swapaxes(weight[::-1, ::-1, ::-1], 3, 4)


def weight_gradient(extended, grad):
    frames, height, width, channels = grad.shape
    spread = jnp.concatenate(
        [extended[:, b : b + height, c : c + width] for b in range(3) for c in range(3)], axis=-1
    )
    taps = [
        lax.dot_general(
            spread[a : a + frames],
            grad,
            (((0, 1, 2), (0, 1, 2)), ((), ())),
            preferred_element_type=jnp.float32,
        )
        for a in range(3)
    ]
    return jnp.stack(taps).reshape(3, 3, 3, channels, channels)


def with_earlier(field):
    frames_here = field.shape[0]
    tail = shifted(field[frames_here - 2 :], "tm", 1)
    return jnp.concatenate([tail, field], axis=0)


def with_later(field):
    head = shifted(field[:2], "tm", -1)
    return jnp.concatenate([field, head], axis=0)


def face_cells(field):
    return extended_2(field, (("row", 1), ("col", 2)), 1)


def local(latent, w_first, b_first, w_second, b_second, upstream, dropout_key):
    frames_here, low_rows, low_cols, channels = latent.shape
    high_rows = 2 * low_rows
    high_cols = 2 * low_cols
    cell_shape = (frames_here, high_rows, high_cols, channels)
    frame_start = lax.axis_index("tm") * frames_here
    row_start = lax.axis_index("row") * high_rows
    col_start = lax.axis_index("col") * high_cols
    height_all = high_rows * lax.axis_size("row")
    width_all = high_cols * lax.axis_size("col")
    latent_ext = with_earlier(latent)
    cells_ext = face_cells(upsample(latent_ext))
    cells_here = cells_ext[2:, 1:-1, 1:-1]
    pre_first = convolve(cells_ext, w_first) + b_first
    scaling = keep_mask(
        dropout_key, frame_start, row_start, col_start, cell_shape, height_all, width_all
    )
    dropped = (jax.nn.silu(pre_first) * scaling).astype(jnp.bfloat16)
    dropped_ext = face_cells(with_earlier(dropped))
    grad_second = weight_gradient(dropped_ext, upstream)
    mixed = (cells_here.astype(jnp.float32) + convolve(dropped_ext, w_second) + b_second).astype(
        jnp.bfloat16
    )
    grad_dropped = convolve(face_cells(with_later(upstream)), flipped(w_second))
    sigma = jax.nn.sigmoid(pre_first)
    grad_pre = (grad_dropped * scaling * sigma * (1.0 + pre_first * (1.0 - sigma))).astype(
        jnp.bfloat16
    )
    grad_first = weight_gradient(cells_ext, grad_pre)
    grad_cells = upstream.astype(jnp.float32) + convolve(
        face_cells(with_later(grad_pre)), flipped(w_first)
    )
    grad_latent = (
        grad_cells.reshape(frames_here, low_rows, 2, low_cols, 2, channels)
        .sum(axis=(2, 4))
        .astype(jnp.bfloat16)
    )
    grad_first, grad_second = lax.psum((grad_first, grad_second), ALL)
    return (mixed, grad_latent, grad_first, grad_second)


def solution(mesh):
    placed = (P("tm", "row", "col", None), P(), P(), P(), P(), P("tm", "row", "col", None), P())
    return jax.shard_map(
        local,
        mesh=mesh,
        in_specs=placed,
        out_specs=(P("tm", "row", "col", None), P("tm", "row", "col", None), P(), P()),
        check_vma=False,
    )
```

```python
import jax
import jax.numpy as jnp
from jax import lax
from jax.sharding import PartitionSpec as P

KEEP_LEVEL = 6554
KEEP_SCALE = 65536.0 / 58982.0
ALL = ("tm", "row", "col")


def shifted(block, axis, distance):
    devices = range(lax.axis_size(axis))
    route = [(i - distance, i) for i in devices if i - distance in devices]
    return lax.ppermute(block, axis, route)


def extended_2(cells, sides, width):
    for axis, dim in sides:
        count = lax.axis_size(axis)
        ends = count - 1
        head = lax.slice_in_dim(cells, 0, width, axis=dim)
        tail = lax.slice_in_dim(cells, cells.shape[dim] - width, cells.shape[dim], axis=dim)
        cells = jnp.concatenate(
            [
                lax.ppermute(tail, axis, [(i, (i + 1) % count) for i in range(ends)]),
                cells,
                lax.ppermute(head, axis, [((i + 1) % count, i) for i in range(ends)]),
            ],
            axis=dim,
        )
    return cells


def keep_mask(dropout_key, frame_start, row_start, col_start, shape, height_all, width_all):
    frame_idx = lax.broadcasted_iota(jnp.int32, shape, 0) + frame_start
    row_idx = lax.broadcasted_iota(jnp.int32, shape, 1) + row_start
    col_idx = lax.broadcasted_iota(jnp.int32, shape, 2) + col_start
    chan_idx = lax.broadcasted_iota(jnp.int32, shape, 3)
    linear = ((frame_idx * height_all + row_idx) * width_all + col_idx) * shape[3] + chan_idx
    state = linear * jnp.int32(-1640531535) + dropout_key[0]
    state = state ^ lax.shift_right_logical(state, jnp.full(shape, 16, jnp.int32))
    state = state * jnp.int32(-2048144789) + dropout_key[1]
    state = state ^ lax.shift_right_logical(state, jnp.full(shape, 13, jnp.int32))
    state = state * jnp.int32(-1028477387)
    state = state ^ lax.shift_right_logical(state, jnp.full(shape, 16, jnp.int32))
    kept = state & 65535 >= KEEP_LEVEL
    return jnp.where(kept, jnp.float32(KEEP_SCALE), jnp.float32(0.0))


def upsample(field):
    return jnp.repeat(jnp.repeat(field, 2, axis=1), 2, axis=2)


def convolve(extended, weight):
    return lax.conv_general_dilated(
        extended[None],
        weight,
        (1, 1, 1),
        "VALID",
        dimension_numbers=("NDHWC", "DHWIO", "NDHWC"),
        preferred_element_type=jnp.float32,
    )[0]


def flipped(weight):
    return jnp.swapaxes(weight[::-1, ::-1, ::-1], 3, 4)


def weight_gradient(extended, grad):
    summed = lax.conv_general_dilated(
        extended[None],
        grad[None],
        (1, 1, 1),
        "VALID",
        dimension_numbers=("CDHWN", "IDHWO", "NDHWC"),
        preferred_element_type=jnp.float32,
    )
    return jnp.transpose(summed, (1, 2, 3, 0, 4))


def with_earlier(field):
    frames_here = field.shape[0]
    tail = shifted(field[frames_here - 2 :], "tm", 1)
    return jnp.concatenate([tail, field], axis=0)


def with_later(field):
    head = shifted(field[:2], "tm", -1)
    return jnp.concatenate([field, head], axis=0)


def face_cells(field):
    return extended_2(field, (("row", 1), ("col", 2)), 1)


def faces_together(fields):
    for axis, dim, other in (("row", 1, 2), ("col", 2, 1)):
        ends = lax.axis_size(axis) - 1
        head = jnp.concatenate([lax.slice_in_dim(f, 0, 1, axis=dim) for f in fields], axis=other)
        tail = jnp.concatenate(
            [lax.slice_in_dim(f, f.shape[dim] - 1, f.shape[dim], axis=dim) for f in fields],
            axis=other,
        )
        from_prev = lax.ppermute(tail, axis, [(i, i + 1) for i in range(ends)])
        from_next = lax.ppermute(head, axis, [(i + 1, i) for i in range(ends)])
        placed = []
        start = 0
        for f in fields:
            size = f.shape[other]
            before = lax.slice_in_dim(from_prev, start, start + size, axis=other)
            after = lax.slice_in_dim(from_next, start, start + size, axis=other)
            placed.append(jnp.concatenate([before, f, after], axis=dim))
            start += size
        fields = placed
    return fields


def local(latent, w_first, b_first, w_second, b_second, upstream, dropout_key):
    frames_here, low_rows, low_cols, channels = latent.shape
    high_rows = 2 * low_rows
    high_cols = 2 * low_cols
    cell_shape = (frames_here, high_rows, high_cols, channels)
    frame_start = lax.axis_index("tm") * frames_here
    row_start = lax.axis_index("row") * high_rows
    col_start = lax.axis_index("col") * high_cols
    height_all = high_rows * lax.axis_size("row")
    width_all = high_cols * lax.axis_size("col")
    latent_ext, upstream_ext = faces_together([with_earlier(latent), with_later(upstream)])
    cells_ext = upsample(latent_ext)[:, 1:-1, 1:-1]
    cells_here = cells_ext[2:, 1:-1, 1:-1]
    pre_first = convolve(cells_ext, w_first) + b_first
    scaling = keep_mask(
        dropout_key, frame_start, row_start, col_start, cell_shape, height_all, width_all
    )
    dropped = (jax.nn.silu(pre_first) * scaling).astype(jnp.bfloat16)
    dropped_ext = face_cells(with_earlier(dropped))
    grad_second = weight_gradient(dropped_ext, upstream)
    mixed = (cells_here.astype(jnp.float32) + convolve(dropped_ext, w_second) + b_second).astype(
        jnp.bfloat16
    )
    grad_dropped = convolve(upstream_ext, flipped(w_second))
    sigma = jax.nn.sigmoid(pre_first)
    grad_pre = (grad_dropped * scaling * sigma * (1.0 + pre_first * (1.0 - sigma))).astype(
        jnp.bfloat16
    )
    grad_first = weight_gradient(cells_ext, grad_pre)
    grad_cells = upstream.astype(jnp.float32) + convolve(
        face_cells(with_later(grad_pre)), flipped(w_first)
    )
    grad_latent = (
        grad_cells.reshape(frames_here, low_rows, 2, low_cols, 2, channels)
        .sum(axis=(2, 4))
        .astype(jnp.bfloat16)
    )
    grad_first, grad_second = lax.psum((grad_first, grad_second), ALL)
    return (mixed, grad_latent, grad_first, grad_second)


def solution(mesh):
    placed = (P("tm", "row", "col", None), P(), P(), P(), P(), P("tm", "row", "col", None), P())
    return jax.shard_map(
        local,
        mesh=mesh,
        in_specs=placed,
        out_specs=(P("tm", "row", "col", None), P("tm", "row", "col", None), P(), P()),
        check_vma=False,
    )
```

```python
import jax
import jax.numpy as jnp
from jax import lax
from jax.sharding import PartitionSpec as P

KEEP_LEVEL = 6554
KEEP_SCALE = 65536.0 / 58982.0
ALL = ("tm", "row", "col")


def shifted(block, axis, distance):
    devices = range(lax.axis_size(axis))
    route = [(i - distance, i) for i in devices if i - distance in devices]
    return lax.ppermute(block, axis, route)


def extended_2(cells, sides, width):
    for axis, dim in sides:
        count = lax.axis_size(axis)
        ends = count - 1
        head = lax.slice_in_dim(cells, 0, width, axis=dim)
        tail = lax.slice_in_dim(cells, cells.shape[dim] - width, cells.shape[dim], axis=dim)
        cells = jnp.concatenate(
            [
                lax.ppermute(tail, axis, [(i, (i + 1) % count) for i in range(ends)]),
                cells,
                lax.ppermute(head, axis, [((i + 1) % count, i) for i in range(ends)]),
            ],
            axis=dim,
        )
    return cells


def keep_mask(dropout_key, frame_start, row_start, col_start, shape, height_all, width_all):
    frame_idx = lax.broadcasted_iota(jnp.int32, shape, 0) + frame_start
    row_idx = lax.broadcasted_iota(jnp.int32, shape, 1) + row_start
    col_idx = lax.broadcasted_iota(jnp.int32, shape, 2) + col_start
    chan_idx = lax.broadcasted_iota(jnp.int32, shape, 3)
    linear = ((frame_idx * height_all + row_idx) * width_all + col_idx) * shape[3] + chan_idx
    state = linear * jnp.int32(-1640531535) + dropout_key[0]
    state = state ^ lax.shift_right_logical(state, jnp.full(shape, 16, jnp.int32))
    state = state * jnp.int32(-2048144789) + dropout_key[1]
    state = state ^ lax.shift_right_logical(state, jnp.full(shape, 13, jnp.int32))
    state = state * jnp.int32(-1028477387)
    state = state ^ lax.shift_right_logical(state, jnp.full(shape, 16, jnp.int32))
    kept = state & 65535 >= KEEP_LEVEL
    return jnp.where(kept, jnp.float32(KEEP_SCALE), jnp.float32(0.0))


def upsample(field):
    return jnp.repeat(jnp.repeat(field, 2, axis=1), 2, axis=2)


def convolve(extended, weight):
    return lax.conv_general_dilated(
        extended[None],
        weight,
        (1, 1, 1),
        "VALID",
        dimension_numbers=("NDHWC", "DHWIO", "NDHWC"),
        preferred_element_type=jnp.float32,
    )[0]


def flipped(weight):
    return jnp.swapaxes(weight[::-1, ::-1, ::-1], 3, 4)


def weight_gradient(extended, grad):
    summed = lax.conv_general_dilated(
        extended[None],
        grad[None],
        (1, 1, 1),
        "VALID",
        dimension_numbers=("CDHWN", "IDHWO", "NDHWC"),
        preferred_element_type=jnp.float32,
    )
    return jnp.transpose(summed, (1, 2, 3, 0, 4))


def with_earlier(field):
    frames_here = field.shape[0]
    tail = shifted(field[frames_here - 2 :], "tm", 1)
    return jnp.concatenate([tail, field], axis=0)


def with_later(field):
    head = shifted(field[:2], "tm", -1)
    return jnp.concatenate([field, head], axis=0)


def face_cells(field):
    return extended_2(field, (("row", 1), ("col", 2)), 1)


def faces_together(fields):
    for axis, dim, other in (("row", 1, 2), ("col", 2, 1)):
        ends = lax.axis_size(axis) - 1
        head = jnp.concatenate([lax.slice_in_dim(f, 0, 1, axis=dim) for f in fields], axis=other)
        tail = jnp.concatenate(
            [lax.slice_in_dim(f, f.shape[dim] - 1, f.shape[dim], axis=dim) for f in fields],
            axis=other,
        )
        from_prev = lax.ppermute(tail, axis, [(i, i + 1) for i in range(ends)])
        from_next = lax.ppermute(head, axis, [(i + 1, i) for i in range(ends)])
        placed = []
        start = 0
        for f in fields:
            size = f.shape[other]
            before = lax.slice_in_dim(from_prev, start, start + size, axis=other)
            after = lax.slice_in_dim(from_next, start, start + size, axis=other)
            placed.append(jnp.concatenate([before, f, after], axis=dim))
            start += size
        fields = placed
    return fields


def local(latent, w_first, b_first, w_second, b_second, upstream, dropout_key):
    frames_here, low_rows, low_cols, channels = latent.shape
    high_rows = 2 * low_rows
    high_cols = 2 * low_cols
    cell_shape = (frames_here, high_rows, high_cols, channels)
    frame_start = lax.axis_index("tm") * frames_here
    row_start = lax.axis_index("row") * high_rows
    col_start = lax.axis_index("col") * high_cols
    height_all = high_rows * lax.axis_size("row")
    width_all = high_cols * lax.axis_size("col")
    latent_ext, upstream_ext = faces_together([with_earlier(latent), with_later(upstream)])
    cells_ext = upsample(latent_ext)[:, 1:-1, 1:-1]
    cells_here = cells_ext[2:, 1:-1, 1:-1]
    pre_first = convolve(cells_ext, w_first) + b_first
    scaling = keep_mask(
        dropout_key, frame_start, row_start, col_start, cell_shape, height_all, width_all
    )
    dropped = (jax.nn.silu(pre_first) * scaling).astype(jnp.bfloat16)
    dropped_ext = face_cells(with_earlier(dropped))
    grad_second = flipped(weight_gradient(upstream_ext, dropped))
    mixed = (cells_here.astype(jnp.float32) + convolve(dropped_ext, w_second) + b_second).astype(
        jnp.bfloat16
    )
    grad_dropped = convolve(upstream_ext, flipped(w_second))
    sigma = jax.nn.sigmoid(pre_first)
    grad_pre = (grad_dropped * scaling * sigma * (1.0 + pre_first * (1.0 - sigma))).astype(
        jnp.bfloat16
    )
    grad_first = weight_gradient(cells_ext, grad_pre)
    grad_cells = upstream.astype(jnp.float32) + convolve(
        face_cells(with_later(grad_pre)), flipped(w_first)
    )
    grad_latent = (
        grad_cells.reshape(frames_here, low_rows, 2, low_cols, 2, channels)
        .sum(axis=(2, 4))
        .astype(jnp.bfloat16)
    )
    grad_first, grad_second = lax.psum((grad_first, grad_second), ALL)
    return (mixed, grad_latent, grad_first, grad_second)


def solution(mesh):
    placed = (P("tm", "row", "col", None), P(), P(), P(), P(), P("tm", "row", "col", None), P())
    return jax.shard_map(
        local,
        mesh=mesh,
        in_specs=placed,
        out_specs=(P("tm", "row", "col", None), P("tm", "row", "col", None), P(), P()),
        check_vma=False,
    )
```

```python
import jax
import jax.numpy as jnp
from jax import lax
from jax.experimental.layout import Layout, with_layout_constraint
from jax.sharding import PartitionSpec as P

KEEP_LEVEL = 6554
KEEP_SCALE = 65536.0 / 58982.0
ALL = ("tm", "row", "col")


def shifted(block, axis, distance):
    devices = range(lax.axis_size(axis))
    route = [(i - distance, i) for i in devices if i - distance in devices]
    return lax.ppermute(block, axis, route)


def extended_2(cells, sides, width):
    for axis, dim in sides:
        count = lax.axis_size(axis)
        ends = count - 1
        head = lax.slice_in_dim(cells, 0, width, axis=dim)
        tail = lax.slice_in_dim(cells, cells.shape[dim] - width, cells.shape[dim], axis=dim)
        cells = jnp.concatenate(
            [
                lax.ppermute(tail, axis, [(i, (i + 1) % count) for i in range(ends)]),
                cells,
                lax.ppermute(head, axis, [((i + 1) % count, i) for i in range(ends)]),
            ],
            axis=dim,
        )
    return cells


def keep_mask(dropout_key, frame_start, row_start, col_start, shape, height_all, width_all):
    frame_idx = lax.broadcasted_iota(jnp.int32, shape, 0) + frame_start
    row_idx = lax.broadcasted_iota(jnp.int32, shape, 1) + row_start
    col_idx = lax.broadcasted_iota(jnp.int32, shape, 2) + col_start
    chan_idx = lax.broadcasted_iota(jnp.int32, shape, 3)
    linear = ((frame_idx * height_all + row_idx) * width_all + col_idx) * shape[3] + chan_idx
    state = linear * jnp.int32(-1640531535) + dropout_key[0]
    state = state ^ lax.shift_right_logical(state, jnp.full(shape, 16, jnp.int32))
    state = state * jnp.int32(-2048144789) + dropout_key[1]
    state = state ^ lax.shift_right_logical(state, jnp.full(shape, 13, jnp.int32))
    state = state * jnp.int32(-1028477387)
    state = state ^ lax.shift_right_logical(state, jnp.full(shape, 16, jnp.int32))
    kept = state & 65535 >= KEEP_LEVEL
    return jnp.where(kept, jnp.float32(KEEP_SCALE), jnp.float32(0.0))


def upsample(field):
    return jnp.repeat(jnp.repeat(field, 2, axis=1), 2, axis=2)


def convolve(extended, weight):
    return lax.conv_general_dilated(
        extended[None],
        weight,
        (1, 1, 1),
        "VALID",
        dimension_numbers=("NDHWC", "DHWIO", "NDHWC"),
        preferred_element_type=jnp.float32,
    )[0]


def flipped(weight):
    return jnp.swapaxes(weight[::-1, ::-1, ::-1], 3, 4)


def weight_gradient(extended, grad):
    summed = lax.conv_general_dilated(
        extended[None],
        grad[None],
        (1, 1, 1),
        "VALID",
        dimension_numbers=("CDHWN", "IDHWO", "NDHWC"),
        preferred_element_type=jnp.float32,
    )
    return jnp.transpose(summed, (1, 2, 3, 0, 4))


def with_earlier(field):
    frames_here = field.shape[0]
    tail = shifted(field[frames_here - 2 :], "tm", 1)
    return jnp.concatenate([tail, field], axis=0)


def with_later(field):
    head = shifted(field[:2], "tm", -1)
    return jnp.concatenate([field, head], axis=0)


def face_cells(field):
    return extended_2(field, (("row", 1), ("col", 2)), 1)


def faces_together(fields):
    for axis, dim, other in (("row", 1, 2), ("col", 2, 1)):
        ends = lax.axis_size(axis) - 1
        head = jnp.concatenate([lax.slice_in_dim(f, 0, 1, axis=dim) for f in fields], axis=other)
        tail = jnp.concatenate(
            [lax.slice_in_dim(f, f.shape[dim] - 1, f.shape[dim], axis=dim) for f in fields],
            axis=other,
        )
        from_prev = lax.ppermute(tail, axis, [(i, i + 1) for i in range(ends)])
        from_next = lax.ppermute(head, axis, [(i + 1, i) for i in range(ends)])
        placed = []
        start = 0
        for f in fields:
            size = f.shape[other]
            before = lax.slice_in_dim(from_prev, start, start + size, axis=other)
            after = lax.slice_in_dim(from_next, start, start + size, axis=other)
            placed.append(jnp.concatenate([before, f, after], axis=dim))
            start += size
        fields = placed
    return fields


def local(latent, w_first, b_first, w_second, b_second, upstream, dropout_key):
    frames_here, low_rows, low_cols, channels = latent.shape
    high_rows = 2 * low_rows
    high_cols = 2 * low_cols
    cell_shape = (frames_here, high_rows, high_cols, channels)
    frame_start = lax.axis_index("tm") * frames_here
    row_start = lax.axis_index("row") * high_rows
    col_start = lax.axis_index("col") * high_cols
    height_all = high_rows * lax.axis_size("row")
    width_all = high_cols * lax.axis_size("col")
    latent_ext, upstream_ext = faces_together([with_earlier(latent), with_later(upstream)])
    cells_ext = upsample(latent_ext)[:, 1:-1, 1:-1]
    cells_here = cells_ext[2:, 1:-1, 1:-1]
    pre_first = convolve(cells_ext, w_first) + b_first
    scaling = keep_mask(
        dropout_key, frame_start, row_start, col_start, cell_shape, height_all, width_all
    )
    dropped = (jax.nn.silu(pre_first) * scaling).astype(jnp.bfloat16)
    dropped_ext = face_cells(with_earlier(dropped))
    grad_second = flipped(weight_gradient(upstream_ext, dropped))
    mixed = (cells_here.astype(jnp.float32) + convolve(dropped_ext, w_second) + b_second).astype(
        jnp.bfloat16
    )
    grad_dropped = convolve(upstream_ext, flipped(w_second))
    sigma = jax.nn.sigmoid(pre_first)
    grad_pre = (grad_dropped * scaling * sigma * (1.0 + pre_first * (1.0 - sigma))).astype(
        jnp.bfloat16
    )
    grad_first = weight_gradient(cells_ext, grad_pre)
    grad_cells = upstream.astype(jnp.float32) + convolve(
        face_cells(with_later(grad_pre)), flipped(w_first)
    )
    grad_latent = (
        grad_cells.reshape(frames_here, low_rows, 2, low_cols, 2, channels)
        .sum(axis=(2, 4))
        .astype(jnp.bfloat16)
    )
    grad_second = with_layout_constraint(grad_second, Layout(major_to_minor=(0, 1, 2, 3, 4)))
    grad_first, grad_second = lax.psum((grad_first, grad_second), ALL)
    return (mixed, grad_latent, grad_first, grad_second)


def solution(mesh):
    placed = (P("tm", "row", "col", None), P(), P(), P(), P(), P("tm", "row", "col", None), P())
    return jax.shard_map(
        local,
        mesh=mesh,
        in_specs=placed,
        out_specs=(P("tm", "row", "col", None), P("tm", "row", "col", None), P(), P()),
        check_vma=False,
    )
```

```python
import jax
import jax.numpy as jnp
from jax import lax
from jax.sharding import PartitionSpec as P

KEEP_LEVEL = 6554
KEEP_SCALE = 65536.0 / 58982.0
ALL = ("tm", "row", "col")


def shifted(block, axis, distance):
    devices = range(lax.axis_size(axis))
    route = [(i - distance, i) for i in devices if i - distance in devices]
    return lax.ppermute(block, axis, route)


def extended_2(cells, sides, width):
    for axis, dim in sides:
        count = lax.axis_size(axis)
        ends = count - 1
        head = lax.slice_in_dim(cells, 0, width, axis=dim)
        tail = lax.slice_in_dim(cells, cells.shape[dim] - width, cells.shape[dim], axis=dim)
        cells = jnp.concatenate(
            [
                lax.ppermute(tail, axis, [(i, (i + 1) % count) for i in range(ends)]),
                cells,
                lax.ppermute(head, axis, [((i + 1) % count, i) for i in range(ends)]),
            ],
            axis=dim,
        )
    return cells


def keep_mask(dropout_key, frame_start, row_start, col_start, shape, height_all, width_all):
    frame_idx = lax.broadcasted_iota(jnp.int32, shape, 0) + frame_start
    row_idx = lax.broadcasted_iota(jnp.int32, shape, 1) + row_start
    col_idx = lax.broadcasted_iota(jnp.int32, shape, 2) + col_start
    chan_idx = lax.broadcasted_iota(jnp.int32, shape, 3)
    linear = ((frame_idx * height_all + row_idx) * width_all + col_idx) * shape[3] + chan_idx
    state = linear * jnp.int32(-1640531535) + dropout_key[0]
    state = state ^ lax.shift_right_logical(state, jnp.full(shape, 16, jnp.int32))
    state = state * jnp.int32(-2048144789) + dropout_key[1]
    state = state ^ lax.shift_right_logical(state, jnp.full(shape, 13, jnp.int32))
    state = state * jnp.int32(-1028477387)
    state = state ^ lax.shift_right_logical(state, jnp.full(shape, 16, jnp.int32))
    kept = state & 65535 >= KEEP_LEVEL
    return jnp.where(kept, jnp.float32(KEEP_SCALE), jnp.float32(0.0))


def upsample(field):
    return jnp.repeat(jnp.repeat(field, 2, axis=1), 2, axis=2)


def convolve(extended, weight):
    return lax.conv_general_dilated(
        extended[None],
        weight,
        (1, 1, 1),
        "VALID",
        dimension_numbers=("NDHWC", "DHWIO", "NDHWC"),
        preferred_element_type=jnp.float32,
    )[0]


def flipped(weight):
    return jnp.swapaxes(weight[::-1, ::-1, ::-1], 3, 4)


def weight_gradient(extended, grad):
    summed = lax.conv_general_dilated(
        extended[None],
        grad[None],
        (1, 1, 1),
        "VALID",
        dimension_numbers=("CDHWN", "IDHWO", "NDHWC"),
        preferred_element_type=jnp.float32,
    )
    return jnp.transpose(summed, (1, 2, 3, 0, 4))


def with_earlier(field):
    frames_here = field.shape[0]
    tail = shifted(field[frames_here - 2 :], "tm", 1)
    return jnp.concatenate([tail, field], axis=0)


def with_later(field):
    head = shifted(field[:2], "tm", -1)
    return jnp.concatenate([field, head], axis=0)


def face_cells(field):
    return extended_2(field, (("row", 1), ("col", 2)), 1)


def faces_together(fields):
    for axis, dim, other in (("row", 1, 2), ("col", 2, 1)):
        ends = lax.axis_size(axis) - 1
        head = jnp.concatenate([lax.slice_in_dim(f, 0, 1, axis=dim) for f in fields], axis=other)
        tail = jnp.concatenate(
            [lax.slice_in_dim(f, f.shape[dim] - 1, f.shape[dim], axis=dim) for f in fields],
            axis=other,
        )
        from_prev = lax.ppermute(tail, axis, [(i, i + 1) for i in range(ends)])
        from_next = lax.ppermute(head, axis, [(i + 1, i) for i in range(ends)])
        placed = []
        start = 0
        for f in fields:
            size = f.shape[other]
            before = lax.slice_in_dim(from_prev, start, start + size, axis=other)
            after = lax.slice_in_dim(from_next, start, start + size, axis=other)
            placed.append(jnp.concatenate([before, f, after], axis=dim))
            start += size
        fields = placed
    return fields


def local(latent, w_first, b_first, w_second, b_second, upstream, dropout_key):
    frames_here, low_rows, low_cols, channels = latent.shape
    high_rows = 2 * low_rows
    high_cols = 2 * low_cols
    cell_shape = (frames_here, high_rows, high_cols, channels)
    frame_start = lax.axis_index("tm") * frames_here
    row_start = lax.axis_index("row") * high_rows
    col_start = lax.axis_index("col") * high_cols
    height_all = high_rows * lax.axis_size("row")
    width_all = high_cols * lax.axis_size("col")
    latent_ext, upstream_ext = faces_together([with_earlier(latent), with_later(upstream)])
    cells_ext = upsample(latent_ext)[:, 1:-1, 1:-1]
    cells_here = cells_ext[2:, 1:-1, 1:-1]
    pre_first = convolve(cells_ext, w_first) + b_first
    scaling = keep_mask(
        dropout_key, frame_start, row_start, col_start, cell_shape, height_all, width_all
    )
    dropped = (jax.nn.silu(pre_first) * scaling).astype(jnp.bfloat16)
    dropped_ext = face_cells(with_earlier(dropped))
    grad_second = jnp.swapaxes(
        weight_gradient(upstream_ext[::-1, ::-1, ::-1], dropped[::-1, ::-1, ::-1]), 3, 4
    )
    mixed = (cells_here.astype(jnp.float32) + convolve(dropped_ext, w_second) + b_second).astype(
        jnp.bfloat16
    )
    grad_dropped = convolve(upstream_ext, flipped(w_second))
    sigma = jax.nn.sigmoid(pre_first)
    grad_pre = (grad_dropped * scaling * sigma * (1.0 + pre_first * (1.0 - sigma))).astype(
        jnp.bfloat16
    )
    grad_first = weight_gradient(cells_ext, grad_pre)
    grad_cells = upstream.astype(jnp.float32) + convolve(
        face_cells(with_later(grad_pre)), flipped(w_first)
    )
    grad_latent = (
        grad_cells.reshape(frames_here, low_rows, 2, low_cols, 2, channels)
        .sum(axis=(2, 4))
        .astype(jnp.bfloat16)
    )
    grad_first, grad_second = lax.psum((grad_first, grad_second), ALL)
    return (mixed, grad_latent, grad_first, grad_second)


def solution(mesh):
    placed = (P("tm", "row", "col", None), P(), P(), P(), P(), P("tm", "row", "col", None), P())
    return jax.shard_map(
        local,
        mesh=mesh,
        in_specs=placed,
        out_specs=(P("tm", "row", "col", None), P("tm", "row", "col", None), P(), P()),
        check_vma=False,
    )
```
